128 devices in a mesh: heads: 4 (over z_lo, core), seq: 32 (over z_hi, x, y).
Axes of the slice: x: 4, y: 4, z: 4 (z_hi: 2, z_lo: 2; z = z_hi * 2 + z_lo), core: 2. Of those that a mesh axis runs over, the one named last changes fastest.
Arguments:
- tokens: bfloat16 [1, 32768, 8192], P(None, 'seq', 'heads'), may hold values from -22 to 22, as said below
- w_query: bfloat16 [8192, 4096], P('seq', 'heads'), may hold values from -0.0625 to 0.0625
- w_key: bfloat16 [8192, 1024], P('seq', 'heads'), may hold values from -0.0625 to 0.0625
- w_value: bfloat16 [8192, 1024], P('seq', 'heads'), may hold values from -0.0625 to 0.0625
- memory_in: float32 [1, 8, 128, 128], P(None, 'heads'), may hold values from -300 to 300, as said below
- norm_in: float32 [1, 8, 128], P(None, 'heads'), may hold values from 16 to 64
- gate_logit: float32 [32], P('heads'), may hold values from -2 to 2
Outputs:
- mixed: bfloat16 [1, 32768, 4096], P(None, 'seq', 'heads')
The draws below stay inside these ranges and needn't reach their ends.
Inputs may be any that keep to these rules, and one draw needn't show every extreme that they name: `tokens`: input activations; every segment of a sequence has its own common component. memory_in[b, g, i, j] equals norm_in[b, g, i] times a factor.
All inputs are finite; a program needn't handle non-finite values.
Results may differ from the reference program's by a relative error of at most 0.0084.
Values may be sent and summed in bfloat16 or wider, within the bound.
No kernel may reach another device: no remote copies, remote signals or barrier semaphores. Data moves between devices by JAX's collectives and lax.ppermute only.
A program may use at most 128 MiB of HBM per device.

```python
import jax
import jax.numpy as jnp
from jax import lax

D = 8192
QH = 32
KVH = 8
HD = 128
SEG = 1024
BATCH = 1
SEQ_LEN = 32768
N_SEQ = 32


def draw_tokens(key, part):
    noise_key, offset_key = jax.random.split(key, 2)
    segments = SEQ_LEN // SEG
    noise = jnp.clip(jax.random.normal(noise_key, (BATCH, segments, SEG, D), jnp.float32), -4.0, 4.0)
    offset = jnp.clip(jax.random.normal(offset_key, (BATCH, segments, 1, D), jnp.float32), -3.0, 3.0)
    base = noise + offset
    return base.reshape(BATCH, SEQ_LEN, D).astype(jnp.bfloat16)


def prior_state(key):
    inner = jax.random.fold_in(key, 7)
    norm_key, common_key, spread_key = jax.random.split(inner, 3)
    norm = jax.random.uniform(norm_key, (BATCH, KVH, HD), jnp.float32, 16.0, 64.0)
    common = jnp.clip(jax.random.normal(common_key, (BATCH, KVH, 1, HD), jnp.float32), -3.0, 3.0)
    spread = jnp.clip(jax.random.normal(spread_key, (BATCH, KVH, HD, HD), jnp.float32), -3.0, 3.0)
    memory = norm[..., None] * (common + 0.5 * spread)
    return (memory, norm)


def draw_memory_in(key, part):
    return prior_state(key)[0]


def draw_norm_in(key, part):
    return prior_state(key)[1]


def block_scale(own_key, dims, cuts, least, largest):
    level, own = 1.0, jax.random.fold_in(own_key, 6)
    for axis_at, shards_of in cuts:
        draws = jnp.exp(jax.random.uniform(jax.random.fold_in(own, axis_at), (shards_of,), jnp.float32, least / len(cuts), largest / len(cuts)))
        level = level * jnp.repeat(draws, dims[axis_at] // shards_of).reshape([-1 if axis == axis_at else 1 for axis in range(len(dims))])
    return level


def centred(own_key, extent, scale, limit, shards=(), kind=jnp.bfloat16):
    loudness = block_scale(own_key, extent, shards, -0.22, 0.18) if shards else 1.0
    values = jax.random.normal(own_key, extent, jnp.float32) * scale * loudness
    return jnp.minimum(jnp.maximum(values, -limit), limit).astype(kind)


def setup_inputs(seed: int = 0) -> dict:
    key_list = jax.random.split(jax.random.key(seed), 8)
    tokens = draw_tokens(jax.random.fold_in(key_list[7], 71), 0)
    w_query = centred(key_list[1], (D, QH * HD), D ** -0.5, 0.0625, ((0, 32), (1, 4)))
    w_key = centred(key_list[2], (D, KVH * HD), D ** -0.5, 0.0625, ((0, 32), (1, 4)))
    w_value = centred(key_list[3], (D, KVH * HD), D ** -0.5, 0.0625, ((0, 32), (1, 4)))
    memory_in = draw_memory_in(jax.random.fold_in(key_list[7], 71), 0)
    norm_in = draw_norm_in(jax.random.fold_in(key_list[7], 71), 0)
    gate_logit = jnp.clip(jax.random.uniform(key_list[6], (QH,), jnp.float32, -2.0, 2.0) * block_scale(key_list[6], (QH,), ((0, 4),), -0.4, 0.0), -2.0, 2.0)
    return {"tokens": tokens, "w_query": w_query, "w_key": w_key, "w_value": w_value, "memory_in": memory_in, "norm_in": norm_in, "gate_logit": gate_logit}


def elu_plus(v):
    return jnp.where(v > 0, v + 1.0, jnp.exp(jnp.minimum(v, 0.0)))


def reference(tokens, w_query, w_key, w_value, memory_in, norm_in, gate_logit):
    group = QH // KVH
    flat = tokens.reshape(BATCH * SEQ_LEN, D)
    queries = jnp.dot(flat, w_query, preferred_element_type=jnp.float32).astype(jnp.bfloat16)
    keys = jnp.dot(flat, w_key, preferred_element_type=jnp.float32).astype(jnp.bfloat16)
    values = jnp.dot(flat, w_value, preferred_element_type=jnp.float32).astype(jnp.bfloat16)
    queries, keys, values = lax.optimization_barrier((queries, keys, values))
    queries = queries.reshape(BATCH, N_SEQ, SEG, KVH, group, HD)
    keys = keys.reshape(BATCH, N_SEQ, SEG, KVH, HD)
    values = values.reshape(BATCH, N_SEQ, SEG, KVH, HD)
    gates = jax.nn.sigmoid(gate_logit).reshape(KVH, group)
    scale = 1.0 / (HD ** 0.5)
    causal = jnp.arange(SEG)[:, None] >= jnp.arange(SEG)[None, :]
    highest = lax.Precision.HIGHEST

    def one(items):
        qb, kb, vb, memory, norm = items
        skall = elu_plus(kb.astype(jnp.float32))
        contrib = jnp.einsum("nsgi,nsgj->ngij", skall, vb.astype(jnp.float32), precision=highest)
        zterm = jnp.sum(skall, axis=1)
        prefix = jnp.cumsum(jnp.concatenate([jnp.zeros((1, KVH, HD, HD), jnp.float32), contrib[:-1]], 0), axis=0)
        zprefix = jnp.cumsum(jnp.concatenate([jnp.zeros((1, KVH, HD), jnp.float32), zterm[:-1]], 0), axis=0)
        mem_all = memory[None] + prefix
        norm_all = norm[None] + zprefix

        def segment(inner):
            qs, ks, vs, mem_s, norm_s = inner
            qf = qs.astype(jnp.float32)
            kf = ks.astype(jnp.float32)
            vf = vs.astype(jnp.float32)
            sq = elu_plus(qf)
            numer = jnp.einsum("sgri,gij->sgrj", sq, mem_s, precision=highest)
            denom = jnp.einsum("sgri,gi->sgr", sq, norm_s, precision=highest)
            retrieved = numer / denom[..., None]
            scores = jnp.einsum("sgrd,tgd->grst", qf, kf) * scale
            scores = jnp.where(causal, scores, -jnp.inf)
            top = jnp.max(scores, axis=-1, keepdims=True)
            expo = jnp.exp(scores - top)
            weights = (expo / jnp.sum(expo, axis=-1, keepdims=True)).astype(jnp.bfloat16)
            weights = lax.optimization_barrier(weights)
            local = jnp.einsum("grst,tgd->sgrd", weights.astype(jnp.float32), vf)
            share = gates[None, :, :, None]
            mixed = share * retrieved + (1.0 - share) * local
            return mixed.astype(jnp.bfloat16).reshape(SEG, QH * HD)

        out = lax.map(segment, (qb, kb, vb, mem_all, norm_all))
        return out.reshape(N_SEQ * SEG, QH * HD)

    return lax.map(one, (queries, keys, values, memory_in, norm_in))
```

```python
import jax
import jax.numpy as jnp
from jax import lax
from jax.sharding import PartitionSpec as P


def elu_plus(v):
    return jnp.where(v > 0, v + 1.0, jnp.exp(jnp.minimum(v, 0.0)))


def swap(x, axis, size, flip):
    return lax.ppermute(x, axis, [(i, i ^ flip) for i in range(size)])


def per_device(tokens, w_query, w_key, w_value, memory_in, norm_in, gate_logit):
    n_heads_dev = 4
    me = lax.axis_index("heads")
    n_seq = lax.axis_size("seq")
    place = lax.axis_index("seq")
    batch, seglen, part = tokens.shape
    kv_heads = memory_in.shape[1]
    head_size = memory_in.shape[2]
    q_heads = gate_logit.shape[0]
    group = q_heads // kv_heads
    qcols = w_query.shape[1]
    kcols = w_key.shape[1]

    wall = jnp.concatenate([w_query, w_key, w_value], axis=1)
    wall = lax.all_gather(wall, "seq", axis=0, tiled=True)

    flat = tokens.reshape(batch * seglen, part)
    cross = swap(flat, "heads", n_heads_dev, 2)
    near = swap(flat, "heads", n_heads_dev, 1)
    far = swap(cross, "heads", n_heads_dev, 1)
    blocks = (flat, near, cross, far)
    acc = None
    for k, blk in enumerate(blocks):
        src = me ^ k
        rows = lax.dynamic_slice_in_dim(wall, src * part, part, axis=0)
        term = jnp.dot(blk, rows, preferred_element_type=jnp.float32)
        acc = term if acc is None else acc + term
    q_acc = acc[:, :qcols]
    k_acc = acc[:, qcols:qcols + kcols]
    v_acc = acc[:, qcols + kcols:]

    keys = k_acc.astype(jnp.bfloat16).reshape(batch, seglen, kv_heads, head_size)
    values = v_acc.astype(jnp.bfloat16).reshape(batch, seglen, kv_heads, head_size)
    highest = lax.Precision.HIGHEST
    sk = elu_plus(keys.astype(jnp.float32))
    contrib = jnp.einsum("bsgi,bsgj->bgij", sk, values.astype(jnp.float32), precision=highest)
    zterm = jnp.sum(sk, axis=1)
    packed = jnp.concatenate([contrib.reshape(-1), zterm.reshape(-1)]).astype(jnp.bfloat16)
    every = lax.all_gather(packed, "seq", axis=0, tiled=False)
    mask = (jnp.arange(n_seq) < place).astype(jnp.float32)
    before = jnp.einsum("s,sn->n", mask, every.astype(jnp.float32), precision=highest)
    nmem = contrib.size
    memory = memory_in + before[:nmem].reshape(contrib.shape)
    znorm = norm_in + before[nmem:].reshape(zterm.shape)

    queries = q_acc.astype(jnp.bfloat16).reshape(batch, seglen, kv_heads, group, head_size)
    scale = 1.0 / head_size**0.5
    causal = jnp.arange(seglen)[:, None] >= jnp.arange(seglen)[None, :]
    shares = jax.nn.sigmoid(gate_logit).reshape(kv_heads, group)

    def per_head(items):
        q_one, k_one, v_one, mem_one, norm_one, share_one = items
        sq = elu_plus(q_one.astype(jnp.float32))
        numer = jnp.einsum("bsri,bij->bsrj", sq, mem_one, precision=highest)
        denom = jnp.einsum("bsri,bi->bsr", sq, norm_one, precision=highest)
        retrieved = numer / denom[..., None]
        scores = (
            jnp.einsum("bsrd,btd->brst", q_one, k_one, preferred_element_type=jnp.float32) * scale
        )
        scores = jnp.where(causal, scores, -jnp.inf)
        top = jnp.max(scores, axis=-1, keepdims=True)
        expo = jnp.exp(scores - top)
        weights = (expo / jnp.sum(expo, axis=-1, keepdims=True)).astype(jnp.bfloat16)
        local = jnp.einsum("brst,btd->bsrd", weights, v_one, preferred_element_type=jnp.float32)
        share = share_one[None, None, :, None]
        return (share * retrieved + (1.0 - share) * local).astype(jnp.bfloat16)

    outputs = lax.map(
        per_head,
        (
            jnp.moveaxis(queries, 2, 0),
            jnp.moveaxis(keys, 2, 0),
            jnp.moveaxis(values, 2, 0),
            jnp.moveaxis(memory, 1, 0),
            jnp.moveaxis(znorm, 1, 0),
            shares,
        ),
    )
    mixed = jnp.moveaxis(outputs, 0, 2)
    return mixed.reshape(batch, seglen, q_heads * head_size)


def solution(mesh):
    in_specs = (
        P(None, "seq", "heads"),
        P("seq", "heads"),
        P("seq", "heads"),
        P("seq", "heads"),
        P(None, "heads", None, None),
        P(None, "heads", None),
        P("heads"),
    )
    out_specs = P(None, "seq", "heads")
    return jax.shard_map(
        per_device, mesh=mesh, in_specs=in_specs, out_specs=out_specs, check_vma=False
    )
```

```python
import jax
import jax.numpy as jnp
from jax import lax
from jax.sharding import PartitionSpec as P


def elu_plus(v):
    return jnp.where(v > 0, v + 1.0, jnp.exp(jnp.minimum(v, 0.0)))


def swap(x, axis, size, flip):
    return lax.ppermute(x, axis, [(i, i ^ flip) for i in range(size)])


def per_device(tokens, w_query, w_key, w_value, memory_in, norm_in, gate_logit):
    n_heads_dev = 4
    me = lax.axis_index("heads")
    n_seq = lax.axis_size("seq")
    place = lax.axis_index("seq")
    batch, seglen, part = tokens.shape
    kv_heads = memory_in.shape[1]
    head_size = memory_in.shape[2]
    q_heads = gate_logit.shape[0]
    group = q_heads // kv_heads
    qcols = w_query.shape[1]
    kcols = w_key.shape[1]

    wall = jnp.concatenate([w_query, w_key, w_value], axis=1)
    wall = lax.all_gather(wall, "seq", axis=0, tiled=True)

    flat = tokens.reshape(batch * seglen, part)
    cross = swap(flat, "heads", n_heads_dev, 2)
    near = swap(flat, "heads", n_heads_dev, 1)
    far = swap(cross, "heads", n_heads_dev, 1)
    blocks = (flat, near, cross, far)
    def project(lo, hi):
        acc = None
        for k, blk in enumerate(blocks):
            src = me ^ k
            rows = lax.dynamic_slice_in_dim(wall[:, lo:hi], src * part, part, axis=0)
            term = jnp.dot(blk, rows, preferred_element_type=jnp.float32)
            acc = term if acc is None else acc + term
        return acc.astype(jnp.bfloat16)

    kv = project(qcols, wall.shape[1])
    keys = kv[:, :kcols].reshape(seglen, kv_heads, head_size)
    values = kv[:, kcols:].reshape(seglen, kv_heads, head_size)
    highest = lax.Precision.HIGHEST
    sk = elu_plus(keys.astype(jnp.float32))
    contrib = jnp.einsum("sgi,sgj->gij", sk, values.astype(jnp.float32), precision=highest)
    zterm = jnp.sum(sk, axis=0)
    packed = jnp.concatenate([contrib.reshape(-1), zterm.reshape(-1)]).astype(jnp.bfloat16)
    every = lax.all_gather(packed, "seq", axis=0, tiled=False)

    queries = project(0, qcols).reshape(seglen, kv_heads, group, head_size)
    scale = 1.0 / head_size**0.5
    causal = jnp.arange(seglen)[:, None] >= jnp.arange(seglen)[None, :]
    shares = jax.nn.sigmoid(gate_logit).reshape(kv_heads, group)

    locals_ = []
    for g in range(kv_heads):
        q_one = queries[:, g]
        scores = jnp.einsum("srd,td->rst", q_one, keys[:, g], preferred_element_type=jnp.float32) * scale
        scores = jnp.where(causal, scores, -jnp.inf)
        top = jnp.max(scores, axis=-1, keepdims=True)
        expo = jnp.exp(scores - top)
        weights = (expo / jnp.sum(expo, axis=-1, keepdims=True)).astype(jnp.bfloat16)
        locals_.append(jnp.einsum("rst,td->srd", weights, values[:, g], preferred_element_type=jnp.float32))

    mask = (jnp.arange(n_seq) < place).astype(jnp.float32)
    before = jnp.einsum("s,sn->n", mask, every.astype(jnp.float32), precision=highest)
    nmem = contrib.size
    memory = memory_in[0] + before[:nmem].reshape(contrib.shape)
    znorm = norm_in[0] + before[nmem:].reshape(zterm.shape)

    outs = []
    for g in range(kv_heads):
        sq = elu_plus(queries[:, g].astype(jnp.float32))
        numer = jnp.einsum("sri,ij->srj", sq, memory[g], precision=highest)
        denom = jnp.einsum("sri,i->sr", sq, znorm[g], precision=highest)
        retrieved = numer / denom[..., None]
        share = shares[g][None, :, None]
        outs.append((share * retrieved + (1.0 - share) * locals_[g]).astype(jnp.bfloat16))
    mixed = jnp.stack(outs, axis=1)
    return mixed.reshape(batch, seglen, q_heads * head_size)


def solution(mesh):
    in_specs = (
        P(None, "seq", "heads"),
        P("seq", "heads"),
        P("seq", "heads"),
        P("seq", "heads"),
        P(None, "heads", None, None),
        P(None, "heads", None),
        P("heads"),
    )
    out_specs = P(None, "seq", "heads")
    return jax.shard_map(
        per_device, mesh=mesh, in_specs=in_specs, out_specs=out_specs, check_vma=False
    )
```

```python
import jax
import jax.numpy as jnp
from jax import lax
from jax.sharding import PartitionSpec as P


def elu_plus(v):
    return jnp.where(v > 0, v + 1.0, jnp.exp(jnp.minimum(v, 0.0)))


def swap(x, axis, size, flip):
    return lax.ppermute(x, axis, [(i, i ^ flip) for i in range(size)])


def per_device(tokens, w_query, w_key, w_value, memory_in, norm_in, gate_logit):
    n_heads_dev = 4
    me = lax.axis_index("heads")
    n_seq = lax.axis_size("seq")
    place = lax.axis_index("seq")
    batch, seglen, part = tokens.shape
    kv_heads = memory_in.shape[1]
    head_size = memory_in.shape[2]
    q_heads = gate_logit.shape[0]
    group = q_heads // kv_heads
    qcols = w_query.shape[1]
    kcols = w_key.shape[1]

    wq_all = lax.all_gather(w_query, "seq", axis=0, tiled=True)
    wkv = jnp.concatenate([w_key, w_value], axis=1)
    rep = jnp.broadcast_to(wkv[None], (n_seq,) + wkv.shape)
    wkv_all = lax.all_to_all(rep, "seq", 0, 0, tiled=True).reshape(-1, wkv.shape[1])

    flat = tokens.reshape(batch * seglen, part)
    cross = swap(flat, "heads", n_heads_dev, 2)
    near = swap(flat, "heads", n_heads_dev, 1)
    far = swap(cross, "heads", n_heads_dev, 1)
    blocks = (flat, near, cross, far)
    def project(wmat):
        acc = None
        for k, blk in enumerate(blocks):
            src = me ^ k
            rows = lax.dynamic_slice_in_dim(wmat, src * part, part, axis=0)
            term = jnp.dot(blk, rows, preferred_element_type=jnp.float32)
            acc = term if acc is None else acc + term
        return acc.astype(jnp.bfloat16)

    kv = project(wkv_all)
    keys = kv[:, :kcols].reshape(seglen, kv_heads, head_size)
    values = kv[:, kcols:].reshape(seglen, kv_heads, head_size)
    highest = lax.Precision.HIGHEST
    sk = elu_plus(keys.astype(jnp.float32))
    contrib = jnp.einsum("sgi,sgj->gij", sk, values.astype(jnp.float32), precision=highest)
    zterm = jnp.sum(sk, axis=0)
    packed = jnp.concatenate([contrib.reshape(-1), zterm.reshape(-1)]).astype(jnp.bfloat16)
    wq_all, packed = lax.optimization_barrier((wq_all, packed))
    every = lax.all_gather(packed, "seq", axis=0, tiled=False)

    queries = project(wq_all).reshape(seglen, kv_heads, group, head_size)
    scale = 1.0 / head_size**0.5
    causal = jnp.arange(seglen)[:, None] >= jnp.arange(seglen)[None, :]
    shares = jax.nn.sigmoid(gate_logit).reshape(kv_heads, group)

    locals_ = []
    for g in range(kv_heads):
        q_one = queries[:, g]
        scores = jnp.einsum("srd,td->rst", q_one, keys[:, g], preferred_element_type=jnp.float32) * scale
        scores = jnp.where(causal, scores, -jnp.inf)
        top = jnp.max(scores, axis=-1, keepdims=True)
        expo = jnp.exp(scores - top)
        weights = (expo / jnp.sum(expo, axis=-1, keepdims=True)).astype(jnp.bfloat16)
        locals_.append(jnp.einsum("rst,td->srd", weights, values[:, g], preferred_element_type=jnp.float32))

    mask = (jnp.arange(n_seq) < place).astype(jnp.float32)
    before = jnp.einsum("s,sn->n", mask, every.astype(jnp.float32), precision=highest)
    nmem = contrib.size
    memory = memory_in[0] + before[:nmem].reshape(contrib.shape)
    znorm = norm_in[0] + before[nmem:].reshape(zterm.shape)

    outs = []
    for g in range(kv_heads):
        sq = elu_plus(queries[:, g].astype(jnp.float32))
        numer = jnp.einsum("sri,ij->srj", sq, memory[g], precision=highest)
        denom = jnp.einsum("sri,i->sr", sq, znorm[g], precision=highest)
        retrieved = numer / denom[..., None]
        share = shares[g][None, :, None]
        outs.append((share * retrieved + (1.0 - share) * locals_[g]).astype(jnp.bfloat16))
    mixed = jnp.stack(outs, axis=1)
    return mixed.reshape(batch, seglen, q_heads * head_size)


def solution(mesh):
    in_specs = (
        P(None, "seq", "heads"),
        P("seq", "heads"),
        P("seq", "heads"),
        P("seq", "heads"),
        P(None, "heads", None, None),
        P(None, "heads", None),
        P("heads"),
    )
    out_specs = P(None, "seq", "heads")
    return jax.shard_map(
        per_device, mesh=mesh, in_specs=in_specs, out_specs=out_specs, check_vma=False
    )
```

```python
import jax
import jax.numpy as jnp
from jax import lax
from jax.sharding import PartitionSpec as P


def elu_plus(v):
    return jnp.where(v > 0, v + 1.0, jnp.exp(jnp.minimum(v, 0.0)))


def swap(x, axis, size, flip):
    return lax.ppermute(x, axis, [(i, i ^ flip) for i in range(size)])


def per_device(tokens, w_query, w_key, w_value, memory_in, norm_in, gate_logit):
    n_heads_dev = 4
    me = lax.axis_index("heads")
    n_seq = lax.axis_size("seq")
    place = lax.axis_index("seq")
    batch, seglen, part = tokens.shape
    kv_heads = memory_in.shape[1]
    head_size = memory_in.shape[2]
    q_heads = gate_logit.shape[0]
    group = q_heads // kv_heads
    qcols = w_query.shape[1]
    kcols = w_key.shape[1]

    wkv = jnp.concatenate([w_key, w_value], axis=1)
    wkv_all = lax.all_gather(wkv, "seq", axis=0, tiled=True)
    flat = tokens.reshape(batch * seglen, part)
    cross = swap(flat, "heads", n_heads_dev, 2)
    near = swap(flat, "heads", n_heads_dev, 1)
    w_query, wkv_all, cross = lax.optimization_barrier((w_query, wkv_all, cross))
    wq_all = lax.all_gather(w_query, "seq", axis=0, tiled=True)

    far = swap(cross, "heads", n_heads_dev, 1)
    blocks = (flat, near, cross, far)
    def project(wmat):
        acc = None
        for k, blk in enumerate(blocks):
            src = me ^ k
            rows = lax.dynamic_slice_in_dim(wmat, src * part, part, axis=0)
            term = jnp.dot(blk, rows, preferred_element_type=jnp.float32)
            acc = term if acc is None else acc + term
        return acc.astype(jnp.bfloat16)

    kv = project(wkv_all)
    keys = kv[:, :kcols].reshape(seglen, kv_heads, head_size)
    values = kv[:, kcols:].reshape(seglen, kv_heads, head_size)
    highest = lax.Precision.HIGHEST
    sk = elu_plus(keys.astype(jnp.float32))
    contrib = jnp.einsum("sgi,sgj->gij", sk, values.astype(jnp.float32), precision=highest)
    zterm = jnp.sum(sk, axis=0)
    packed = jnp.concatenate([contrib.reshape(-1), zterm.reshape(-1)])
    total = packed
    step = 1
    while step < n_seq:
        total = total + lax.ppermute(total, "seq", [(i, i + step) for i in range(n_seq - step)])
        step *= 2
    before = total - packed

    queries = project(wq_all).reshape(seglen, kv_heads, group, head_size)
    scale = 1.0 / head_size**0.5
    causal = jnp.arange(seglen)[:, None] >= jnp.arange(seglen)[None, :]
    shares = jax.nn.sigmoid(gate_logit).reshape(kv_heads, group)

    locals_ = []
    for g in range(kv_heads):
        q_one = queries[:, g]
        scores = jnp.einsum("srd,td->rst", q_one, keys[:, g], preferred_element_type=jnp.float32) * scale
        scores = jnp.where(causal, scores, -jnp.inf)
        top = jnp.max(scores, axis=-1, keepdims=True)
        expo = jnp.exp(scores - top)
        weights = (expo / jnp.sum(expo, axis=-1, keepdims=True)).astype(jnp.bfloat16)
        locals_.append(jnp.einsum("rst,td->srd", weights, values[:, g], preferred_element_type=jnp.float32))

    nmem = contrib.size
    memory = memory_in[0] + before[:nmem].reshape(contrib.shape)
    znorm = norm_in[0] + before[nmem:].reshape(zterm.shape)

    outs = []
    for g in range(kv_heads):
        sq = elu_plus(queries[:, g].astype(jnp.float32))
        numer = jnp.einsum("sri,ij->srj", sq, memory[g], precision=highest)
        denom = jnp.einsum("sri,i->sr", sq, znorm[g], precision=highest)
        retrieved = numer / denom[..., None]
        share = shares[g][None, :, None]
        outs.append((share * retrieved + (1.0 - share) * locals_[g]).astype(jnp.bfloat16))
    mixed = jnp.stack(outs, axis=1)
    return mixed.reshape(batch, seglen, q_heads * head_size)


def solution(mesh):
    in_specs = (
        P(None, "seq", "heads"),
        P("seq", "heads"),
        P("seq", "heads"),
        P("seq", "heads"),
        P(None, "heads", None, None),
        P(None, "heads", None),
        P("heads"),
    )
    out_specs = P(None, "seq", "heads")
    return jax.shard_map(
        per_device, mesh=mesh, in_specs=in_specs, out_specs=out_specs, check_vma=False
    )
```

```python
import jax
import jax.numpy as jnp
from jax import lax
from jax.sharding import PartitionSpec as P


def elu_plus(v):
    return jnp.where(v > 0, v + 1.0, jnp.exp(jnp.minimum(v, 0.0)))


def swap(x, axis, size, flip):
    return lax.ppermute(x, axis, [(i, i ^ flip) for i in range(size)])


def per_device(tokens, w_query, w_key, w_value, memory_in, norm_in, gate_logit):
    n_heads_dev = 4
    me = lax.axis_index("heads")
    n_seq = lax.axis_size("seq")
    batch, seglen, part = tokens.shape
    kv_heads = memory_in.shape[1]
    head_size = memory_in.shape[2]
    q_heads = gate_logit.shape[0]
    group = q_heads // kv_heads
    kcols = w_key.shape[1]
    width = group * head_size

    stack = [w_query[:, g * width:(g + 1) * width] for g in range(kv_heads)]
    stack.append(jnp.concatenate([w_key, w_value], axis=1))
    wall = lax.all_gather(jnp.stack(stack), "seq", axis=1, tiled=True)

    flat = tokens.reshape(batch * seglen, part)
    cross = swap(flat, "heads", n_heads_dev, 2)
    near = swap(flat, "heads", n_heads_dev, 1)
    far = swap(cross, "heads", n_heads_dev, 1)
    blocks = (flat, near, cross, far)

    def project(wmat):
        acc = None
        for k, blk in enumerate(blocks):
            rows = lax.dynamic_slice_in_dim(wmat, (me ^ k) * part, part, axis=0)
            term = jnp.dot(blk, rows, preferred_element_type=jnp.float32)
            acc = term if acc is None else acc + term
        return acc.astype(jnp.bfloat16)

    kv = project(wall[kv_heads])
    keys = kv[:, :kcols].reshape(seglen, kv_heads, head_size)
    values = kv[:, kcols:].reshape(seglen, kv_heads, head_size)
    highest = lax.Precision.HIGHEST
    sk = elu_plus(keys.astype(jnp.float32))
    contrib = jnp.einsum("sgi,sgj->gij", sk, values.astype(jnp.float32), precision=highest)
    zterm = jnp.sum(sk, axis=0)

    packed = jnp.concatenate([contrib.reshape(-1), zterm.reshape(-1)])
    total = packed
    step = 1
    while step < n_seq:
        total = total + lax.ppermute(total, "seq", [(i, i + step) for i in range(n_seq - step)])
        step *= 2
    before = total - packed
    nmem = contrib.size
    memory = memory_in[0] + before[:nmem].reshape(contrib.shape)
    znorm = norm_in[0] + before[nmem:].reshape(zterm.shape)

    scale = 1.0 / head_size**0.5
    causal = jnp.arange(seglen)[:, None] >= jnp.arange(seglen)[None, :]
    shares = jax.nn.sigmoid(gate_logit).reshape(kv_heads, group)
    high = lax.Precision.HIGH

    outs = []
    for g in range(kv_heads):
        q_one = project(wall[g]).reshape(seglen, group, head_size)
        scores = jnp.einsum("srd,td->rst", q_one, keys[:, g], preferred_element_type=jnp.float32) * scale
        scores = jnp.where(causal, scores, -jnp.inf)
        top = jnp.max(scores, axis=-1, keepdims=True)
        expo = jnp.exp(scores - top)
        weights = (expo / jnp.sum(expo, axis=-1, keepdims=True)).astype(jnp.bfloat16)
        local = jnp.einsum("rst,td->srd", weights, values[:, g], preferred_element_type=jnp.float32)
        sq = elu_plus(q_one.astype(jnp.float32))
        numer = jnp.einsum("sri,ij->srj", sq, memory[g], precision=high)
        denom = jnp.einsum("sri,i->sr", sq, znorm[g], precision=high)
        retrieved = numer / denom[..., None]
        share = shares[g][None, :, None]
        outs.append((share * retrieved + (1.0 - share) * local).astype(jnp.bfloat16))
    mixed = jnp.stack(outs, axis=1)
    return mixed.reshape(batch, seglen, q_heads * head_size)


def solution(mesh):
    in_specs = (
        P(None, "seq", "heads"),
        P("seq", "heads"),
        P("seq", "heads"),
        P("seq", "heads"),
        P(None, "heads", None, None),
        P(None, "heads", None),
        P("heads"),
    )
    out_specs = P(None, "seq", "heads")
    return jax.shard_map(
        per_device, mesh=mesh, in_specs=in_specs, out_specs=out_specs, check_vma=False
    )
```

```python
import jax
import jax.numpy as jnp
from jax import lax
from jax.sharding import PartitionSpec as P


def elu_plus(v):
    return jnp.where(v > 0, v + 1.0, jnp.exp(jnp.minimum(v, 0.0)))


def swap(x, axis, size, flip):
    return lax.ppermute(x, axis, [(i, i ^ flip) for i in range(size)])


def per_device(tokens, w_query, w_key, w_value, memory_in, norm_in, gate_logit):
    n_heads_dev = 4
    me = lax.axis_index("heads")
    n_seq = lax.axis_size("seq")
    place = lax.axis_index("seq")
    batch, seglen, part = tokens.shape
    kv_heads = memory_in.shape[1]
    head_size = memory_in.shape[2]
    q_heads = gate_logit.shape[0]
    group = q_heads // kv_heads
    qcols = w_query.shape[1]
    kcols = w_key.shape[1]

    wall = jnp.concatenate([w_query, w_key, w_value], axis=1)
    wall = lax.all_gather(wall, "seq", axis=0, tiled=True)

    flat = tokens.reshape(batch * seglen, part)
    cross = swap(flat, "heads", n_heads_dev, 2)
    near = swap(flat, "heads", n_heads_dev, 1)
    far = swap(cross, "heads", n_heads_dev, 1)
    blocks = (flat, near, cross, far)
    acc = None
    for k, blk in enumerate(blocks):
        rows = lax.dynamic_slice_in_dim(wall, (me ^ k) * part, part, axis=0)
        term = jnp.dot(blk, rows, preferred_element_type=jnp.float32)
        acc = term if acc is None else acc + term
    proj = acc.astype(jnp.bfloat16)
    keys = proj[:, qcols:qcols + kcols].reshape(seglen, kv_heads, head_size)
    values = proj[:, qcols + kcols:].reshape(seglen, kv_heads, head_size)
    highest = lax.Precision.HIGHEST
    sk = elu_plus(keys.astype(jnp.float32))
    contrib = jnp.einsum("sgi,sgj->gij", sk, values.astype(jnp.float32), precision=highest)
    zterm = jnp.sum(sk, axis=0)
    packed = jnp.concatenate([contrib.reshape(-1), zterm.reshape(-1)]).astype(jnp.bfloat16)
    every = lax.all_gather(packed, "seq", axis=0, tiled=False)

    queries = proj[:, :qcols].reshape(seglen, kv_heads, group, head_size)
    scale = 1.0 / head_size**0.5
    causal = jnp.arange(seglen)[:, None] >= jnp.arange(seglen)[None, :]
    shares = jax.nn.sigmoid(gate_logit).reshape(kv_heads, group)

    locals_ = []
    for g in range(kv_heads):
        q_one = queries[:, g]
        scores = jnp.einsum("srd,td->rst", q_one, keys[:, g], preferred_element_type=jnp.float32) * scale
        scores = jnp.where(causal, scores, -jnp.inf)
        top = jnp.max(scores, axis=-1, keepdims=True)
        expo = jnp.exp(scores - top)
        weights = (expo / jnp.sum(expo, axis=-1, keepdims=True)).astype(jnp.bfloat16)
        locals_.append(jnp.einsum("rst,td->srd", weights, values[:, g], preferred_element_type=jnp.float32))

    mask = (jnp.arange(n_seq) < place).astype(jnp.float32)
    before = jnp.einsum("s,sn->n", mask, every.astype(jnp.float32), precision=highest)
    nmem = contrib.size
    memory = memory_in[0] + before[:nmem].reshape(contrib.shape)
    znorm = norm_in[0] + before[nmem:].reshape(zterm.shape)

    outs = []
    for g in range(kv_heads):
        sq = elu_plus(queries[:, g].astype(jnp.float32))
        numer = jnp.einsum("sri,ij->srj", sq, memory[g], precision=lax.Precision.HIGH)
        denom = jnp.einsum("sri,i->sr", sq, znorm[g], precision=lax.Precision.HIGH)
        retrieved = numer / denom[..., None]
        share = shares[g][None, :, None]
        outs.append((share * retrieved + (1.0 - share) * locals_[g]).astype(jnp.bfloat16))
    mixed = jnp.stack(outs, axis=1)
    return mixed.reshape(batch, seglen, q_heads * head_size)


def solution(mesh):
    in_specs = (
        P(None, "seq", "heads"),
        P("seq", "heads"),
        P("seq", "heads"),
        P("seq", "heads"),
        P(None, "heads", None, None),
        P(None, "heads", None),
        P("heads"),
    )
    out_specs = P(None, "seq", "heads")
    return jax.shard_map(
        per_device, mesh=mesh, in_specs=in_specs, out_specs=out_specs, check_vma=False
    )
```

```python
import jax
import jax.numpy as jnp
from jax import lax
from jax.sharding import PartitionSpec as P


def elu_plus(v):
    return jnp.where(v > 0, v + 1.0, jnp.exp(jnp.minimum(v, 0.0)))


def swap(x, axis, size, flip):
    return lax.ppermute(x, axis, [(i, i ^ flip) for i in range(size)])


def per_device(tokens, w_query, w_key, w_value, memory_in, norm_in, gate_logit):
    n_heads_dev = 4
    me = lax.axis_index("heads")
    n_seq = lax.axis_size("seq")
    place = lax.axis_index("seq")
    batch, seglen, part = tokens.shape
    kv_heads = memory_in.shape[1]
    head_size = memory_in.shape[2]
    q_heads = gate_logit.shape[0]
    group = q_heads // kv_heads
    qcols = w_query.shape[1]
    kcols = w_key.shape[1]

    wall = jnp.concatenate([w_query, w_key, w_value], axis=1)
    wall = lax.all_gather(wall, "seq", axis=0, tiled=True)

    flat = tokens.reshape(batch * seglen, part)
    cross = swap(flat, "heads", n_heads_dev, 2)
    near = swap(flat, "heads", n_heads_dev, 1)
    far = swap(cross, "heads", n_heads_dev, 1)
    blocks = (flat, near, cross, far)
    def project(lo, hi):
        acc = None
        for k, blk in enumerate(blocks):
            src = me ^ k
            rows = lax.dynamic_slice(wall, (src * part, lo), (part, hi - lo))
            term = jnp.dot(blk, rows, preferred_element_type=jnp.float32)
            acc = term if acc is None else acc + term
        return acc.astype(jnp.bfloat16)

    kv = project(qcols, wall.shape[1])
    keys = kv[:, :kcols].reshape(seglen, kv_heads, head_size)
    values = kv[:, kcols:].reshape(seglen, kv_heads, head_size)
    highest = lax.Precision.HIGHEST
    sk = elu_plus(keys.astype(jnp.float32))
    contrib = jnp.einsum("sgi,sgj->gij", sk, values.astype(jnp.float32), precision=highest)
    zterm = jnp.sum(sk, axis=0)
    packed = jnp.concatenate([contrib.reshape(-1), zterm.reshape(-1)]).astype(jnp.bfloat16)
    every = lax.all_gather(packed, "seq", axis=0, tiled=False)

    queries = project(0, qcols).reshape(seglen, kv_heads, group, head_size)
    scale = 1.0 / head_size**0.5
    causal = jnp.arange(seglen)[:, None] >= jnp.arange(seglen)[None, :]
    shares = jax.nn.sigmoid(gate_logit).reshape(kv_heads, group)

    locals_ = []
    for g in range(kv_heads):
        q_one = queries[:, g]
        scores = jnp.einsum("srd,td->rst", q_one, keys[:, g], preferred_element_type=jnp.float32) * scale
        scores = jnp.where(causal, scores, -jnp.inf)
        top = jnp.max(scores, axis=-1, keepdims=True)
        expo = jnp.exp(scores - top)
        weights = (expo / jnp.sum(expo, axis=-1, keepdims=True)).astype(jnp.bfloat16)
        locals_.append(jnp.einsum("rst,td->srd", weights, values[:, g], preferred_element_type=jnp.float32))

    mask = (jnp.arange(n_seq) < place).astype(jnp.float32)
    before = jnp.einsum("s,sn->n", mask, every.astype(jnp.float32), precision=highest)
    nmem = contrib.size
    memory = memory_in[0] + before[:nmem].reshape(contrib.shape)
    znorm = norm_in[0] + before[nmem:].reshape(zterm.shape)

    outs = []
    for g in range(kv_heads):
        sq = elu_plus(queries[:, g].astype(jnp.float32))
        numer = jnp.einsum("sri,ij->srj", sq, memory[g], precision=lax.Precision.HIGH)
        denom = jnp.einsum("sri,i->sr", sq, znorm[g], precision=lax.Precision.HIGH)
        retrieved = numer / denom[..., None]
        share = shares[g][None, :, None]
        outs.append((share * retrieved + (1.0 - share) * locals_[g]).astype(jnp.bfloat16))
    mixed = jnp.stack(outs, axis=1)
    return mixed.reshape(batch, seglen, q_heads * head_size)


def solution(mesh):
    in_specs = (
        P(None, "seq", "heads"),
        P("seq", "heads"),
        P("seq", "heads"),
        P("seq", "heads"),
        P(None, "heads", None, None),
        P(None, "heads", None),
        P("heads"),
    )
    out_specs = P(None, "seq", "heads")
    return jax.shard_map(
        per_device, mesh=mesh, in_specs=in_specs, out_specs=out_specs, check_vma=False
    )
```

```python
import jax
import jax.numpy as jnp
from jax import lax
from jax.sharding import PartitionSpec as P


def elu_plus(v):
    return jnp.where(v > 0, v + 1.0, jnp.exp(jnp.minimum(v, 0.0)))


def swap(x, axis, size, flip):
    return lax.ppermute(x, axis, [(i, i ^ flip) for i in range(size)])


def per_device(tokens, w_query, w_key, w_value, memory_in, norm_in, gate_logit):
    n_heads_dev = 4
    me = lax.axis_index("heads")
    n_seq = lax.axis_size("seq")
    place = lax.axis_index("seq")
    batch, seglen, part = tokens.shape
    kv_heads = memory_in.shape[1]
    head_size = memory_in.shape[2]
    q_heads = gate_logit.shape[0]
    group = q_heads // kv_heads
    qcols = w_query.shape[1]
    kcols = w_key.shape[1]

    wall = jnp.concatenate([w_query, w_key, w_value], axis=1)
    wall = lax.all_gather(wall, "seq", axis=0, tiled=True)

    flat = tokens.reshape(batch * seglen, part)
    cross = swap(flat, "heads", n_heads_dev, 2)
    near = swap(flat, "heads", n_heads_dev, 1)
    far = swap(cross, "heads", n_heads_dev, 1)
    blocks = (flat, near, cross, far)
    def project(lo, hi):
        acc = None
        for k, blk in enumerate(blocks):
            src = me ^ k
            rows = lax.dynamic_slice(wall, (src * part, lo), (part, hi - lo))
            term = jnp.dot(blk, rows, preferred_element_type=jnp.float32)
            acc = term if acc is None else acc + term
        return acc.astype(jnp.bfloat16)

    kv = project(qcols, wall.shape[1])
    keys = kv[:, :kcols].reshape(seglen, kv_heads, head_size)
    values = kv[:, kcols:].reshape(seglen, kv_heads, head_size)
    highest = lax.Precision.HIGHEST
    sk = elu_plus(keys.astype(jnp.float32))
    contrib = jnp.einsum("sgi,sgj->gij", sk, values.astype(jnp.float32), precision=highest)
    zterm = jnp.sum(sk, axis=0)
    packed = jnp.concatenate([contrib.reshape(-1), zterm.reshape(-1)]).astype(jnp.bfloat16)
    packed, wall = lax.optimization_barrier((packed, wall))
    every = lax.all_gather(packed, "seq", axis=0, tiled=False)

    queries = project(0, qcols).reshape(seglen, kv_heads, group, head_size)
    scale = 1.0 / head_size**0.5
    causal = jnp.arange(seglen)[:, None] >= jnp.arange(seglen)[None, :]
    shares = jax.nn.sigmoid(gate_logit).reshape(kv_heads, group)

    locals_ = []
    for g in range(kv_heads):
        q_one = queries[:, g]
        scores = jnp.einsum("srd,td->rst", q_one, keys[:, g], preferred_element_type=jnp.float32) * scale
        scores = jnp.where(causal, scores, -jnp.inf)
        top = jnp.max(scores, axis=-1, keepdims=True)
        expo = jnp.exp(scores - top)
        weights = (expo / jnp.sum(expo, axis=-1, keepdims=True)).astype(jnp.bfloat16)
        locals_.append(jnp.einsum("rst,td->srd", weights, values[:, g], preferred_element_type=jnp.float32))

    every, locals_ = lax.optimization_barrier((every, locals_))
    mask = (jnp.arange(n_seq) < place).astype(jnp.float32)
    before = jnp.einsum("s,sn->n", mask, every.astype(jnp.float32), precision=highest)
    nmem = contrib.size
    memory = memory_in[0] + before[:nmem].reshape(contrib.shape)
    znorm = norm_in[0] + before[nmem:].reshape(zterm.shape)

    outs = []
    for g in range(kv_heads):
        sq = elu_plus(queries[:, g].astype(jnp.float32))
        numer = jnp.einsum("sri,ij->srj", sq, memory[g], precision=lax.Precision.HIGH)
        denom = jnp.einsum("sri,i->sr", sq, znorm[g], precision=lax.Precision.HIGH)
        retrieved = numer / denom[..., None]
        share = shares[g][None, :, None]
        outs.append((share * retrieved + (1.0 - share) * locals_[g]).astype(jnp.bfloat16))
    mixed = jnp.stack(outs, axis=1)
    return mixed.reshape(batch, seglen, q_heads * head_size)


def solution(mesh):
    in_specs = (
        P(None, "seq", "heads"),
        P("seq", "heads"),
        P("seq", "heads"),
        P("seq", "heads"),
        P(None, "heads", None, None),
        P(None, "heads", None),
        P("heads"),
    )
    out_specs = P(None, "seq", "heads")
    return jax.shard_map(
        per_device, mesh=mesh, in_specs=in_specs, out_specs=out_specs, check_vma=False
    )
```

```python
import jax
import jax.numpy as jnp
from jax import lax
from jax.sharding import PartitionSpec as P


def elu_plus(v):
    return jnp.where(v > 0, v + 1.0, jnp.exp(jnp.minimum(v, 0.0)))


def swap(x, axis, size, flip):
    return lax.ppermute(x, axis, [(i, i ^ flip) for i in range(size)])


def per_device(tokens, w_query, w_key, w_value, memory_in, norm_in, gate_logit):
    n_heads_dev = 4
    me = lax.axis_index("heads")
    n_seq = lax.axis_size("seq")
    place = lax.axis_index("seq")
    batch, seglen, part = tokens.shape
    kv_heads = memory_in.shape[1]
    head_size = memory_in.shape[2]
    q_heads = gate_logit.shape[0]
    group = q_heads // kv_heads
    qcols = w_query.shape[1]
    kcols = w_key.shape[1]

    wall = jnp.concatenate([w_query, w_key, w_value], axis=1)
    wall = lax.all_gather(wall, "seq", axis=0, tiled=True)

    flat = tokens.reshape(batch * seglen, part)
    cross = swap(flat, "heads", n_heads_dev, 2)
    near = swap(flat, "heads", n_heads_dev, 1)
    far = swap(cross, "heads", n_heads_dev, 1)
    blocks = (flat, near, cross, far)
    full = jnp.zeros((batch * seglen, n_heads_dev * part), flat.dtype)
    for k, blk in enumerate(blocks):
        full = lax.dynamic_update_slice(full, blk, (0, (me ^ k) * part))
    zero = me // n_heads_dev

    def project(lo, hi):
        rows = lax.dynamic_slice(wall, (zero, lo + zero), (wall.shape[0], hi - lo))
        return jnp.dot(full, rows, preferred_element_type=jnp.float32).astype(jnp.bfloat16)

    kv = project(qcols, wall.shape[1])
    keys = kv[:, :kcols].reshape(seglen, kv_heads, head_size)
    values = kv[:, kcols:].reshape(seglen, kv_heads, head_size)
    highest = lax.Precision.HIGHEST
    sk = elu_plus(keys.astype(jnp.float32))
    contrib = jnp.einsum("sgi,sgj->gij", sk, values.astype(jnp.float32), precision=highest)
    zterm = jnp.sum(sk, axis=0)
    packed = jnp.concatenate([contrib.reshape(-1), zterm.reshape(-1)]).astype(jnp.bfloat16)
    packed, wall = lax.optimization_barrier((packed, wall))
    every = lax.all_gather(packed, "seq", axis=0, tiled=False)

    queries = project(0, qcols).reshape(seglen, kv_heads, group, head_size)
    scale = 1.0 / head_size**0.5
    causal = jnp.arange(seglen)[:, None] >= jnp.arange(seglen)[None, :]
    shares = jax.nn.sigmoid(gate_logit).reshape(kv_heads, group)

    locals_ = []
    for g in range(kv_heads):
        q_one = queries[:, g]
        scores = jnp.einsum("srd,td->rst", q_one, keys[:, g], preferred_element_type=jnp.float32) * scale
        scores = jnp.where(causal, scores, -jnp.inf)
        top = jnp.max(scores, axis=-1, keepdims=True)
        expo = jnp.exp(scores - top)
        weights = (expo / jnp.sum(expo, axis=-1, keepdims=True)).astype(jnp.bfloat16)
        locals_.append(jnp.einsum("rst,td->srd", weights, values[:, g], preferred_element_type=jnp.float32))

    every, locals_ = lax.optimization_barrier((every, locals_))
    mask = (jnp.arange(n_seq) < place).astype(jnp.float32)
    before = jnp.einsum("s,sn->n", mask, every.astype(jnp.float32), precision=highest)
    nmem = contrib.size
    memory = memory_in[0] + before[:nmem].reshape(contrib.shape)
    znorm = norm_in[0] + before[nmem:].reshape(zterm.shape)

    outs = []
    for g in range(kv_heads):
        sq = elu_plus(queries[:, g].astype(jnp.float32))
        numer = jnp.einsum("sri,ij->srj", sq, memory[g], precision=lax.Precision.HIGH)
        denom = jnp.einsum("sri,i->sr", sq, znorm[g], precision=lax.Precision.HIGH)
        retrieved = numer / denom[..., None]
        share = shares[g][None, :, None]
        outs.append((share * retrieved + (1.0 - share) * locals_[g]).astype(jnp.bfloat16))
    mixed = jnp.stack(outs, axis=1)
    return mixed.reshape(batch, seglen, q_heads * head_size)


def solution(mesh):
    in_specs = (
        P(None, "seq", "heads"),
        P("seq", "heads"),
        P("seq", "heads"),
        P("seq", "heads"),
        P(None, "heads", None, None),
        P(None, "heads", None),
        P("heads"),
    )
    out_specs = P(None, "seq", "heads")
    return jax.shard_map(
        per_device, mesh=mesh, in_specs=in_specs, out_specs=out_specs, check_vma=False
    )
```

```python
import jax
import jax.numpy as jnp
from jax import lax
from jax.sharding import PartitionSpec as P


def elu_plus(v):
    return jnp.where(v > 0, v + 1.0, jnp.exp(jnp.minimum(v, 0.0)))


def swap(x, axis, size, flip):
    return lax.ppermute(x, axis, [(i, i ^ flip) for i in range(size)])


def per_device(tokens, w_query, w_key, w_value, memory_in, norm_in, gate_logit):
    n_heads_dev = 4
    me = lax.axis_index("heads")
    n_seq = lax.axis_size("seq")
    place = lax.axis_index("seq")
    batch, seglen, part = tokens.shape
    kv_heads = memory_in.shape[1]
    head_size = memory_in.shape[2]
    q_heads = gate_logit.shape[0]
    group = q_heads // kv_heads
    qcols = w_query.shape[1]
    kcols = w_key.shape[1]

    wall = jnp.concatenate([w_query, w_key, w_value], axis=1)
    wall = lax.all_gather(wall, "seq", axis=0, tiled=True)

    flat = tokens.reshape(batch * seglen, part)
    cross = swap(flat, "heads", n_heads_dev, 2)
    near = swap(flat, "heads", n_heads_dev, 1)
    far = swap(cross, "heads", n_heads_dev, 1)
    blocks = (flat, near, cross, far)
    full = jnp.zeros((batch * seglen, n_heads_dev * part), flat.dtype)
    for k, blk in enumerate(blocks):
        full = lax.dynamic_update_slice(full, blk, (0, (me ^ k) * part))
    zero = me // n_heads_dev

    def project(lo, hi):
        rows = lax.dynamic_slice(wall, (zero, lo + zero), (wall.shape[0], hi - lo))
        return jnp.dot(full, rows, preferred_element_type=jnp.float32).astype(jnp.bfloat16)

    kv = project(qcols, wall.shape[1])
    keys = kv[:, :kcols].reshape(seglen, kv_heads, head_size)
    values = kv[:, kcols:].reshape(seglen, kv_heads, head_size)
    highest = lax.Precision.HIGHEST
    sk = elu_plus(keys.astype(jnp.float32))
    contrib = jnp.einsum("sgi,sgj->gij", sk, values.astype(jnp.float32), precision=highest)
    zterm = jnp.sum(sk, axis=0)
    packed = jnp.concatenate([contrib.reshape(-1), zterm.reshape(-1)]).astype(jnp.bfloat16)
    packed, wall = lax.optimization_barrier((packed, wall))
    every = lax.all_gather(packed, "seq", axis=0, tiled=False)

    queries = project(0, qcols).reshape(seglen, kv_heads, group, head_size)
    scale = 1.0 / head_size**0.5
    causal = jnp.arange(seglen)[:, None] >= jnp.arange(seglen)[None, :]
    shares = jax.nn.sigmoid(gate_logit).reshape(kv_heads, group)

    qf = queries
    scores = jnp.einsum("sgrd,tgd->grst", qf, keys, preferred_element_type=jnp.float32) * scale
    scores = jnp.where(causal, scores, -jnp.inf)
    top = jnp.max(scores, axis=-1, keepdims=True)
    expo = jnp.exp(scores - top)
    weights = (expo / jnp.sum(expo, axis=-1, keepdims=True)).astype(jnp.bfloat16)
    local = jnp.einsum("grst,tgd->sgrd", weights, values, preferred_element_type=jnp.float32)

    every, local = lax.optimization_barrier((every, local))
    mask = (jnp.arange(n_seq) < place).astype(jnp.float32)
    before = jnp.einsum("s,sn->n", mask, every.astype(jnp.float32), precision=highest)
    nmem = contrib.size
    memory = memory_in[0] + before[:nmem].reshape(contrib.shape)
    znorm = norm_in[0] + before[nmem:].reshape(zterm.shape)

    high = lax.Precision.HIGH
    sq = elu_plus(queries.astype(jnp.float32))
    numer = jnp.einsum("sgri,gij->sgrj", sq, memory, precision=high)
    denom = jnp.einsum("sgri,gi->sgr", sq, znorm, precision=high)
    retrieved = numer / denom[..., None]
    share = shares[None, :, :, None]
    mixed = (share * retrieved + (1.0 - share) * local).astype(jnp.bfloat16)
    return mixed.reshape(batch, seglen, q_heads * head_size)


def solution(mesh):
    in_specs = (
        P(None, "seq", "heads"),
        P("seq", "heads"),
        P("seq", "heads"),
        P("seq", "heads"),
        P(None, "heads", None, None),
        P(None, "heads", None),
        P("heads"),
    )
    out_specs = P(None, "seq", "heads")
    return jax.shard_map(
        per_device, mesh=mesh, in_specs=in_specs, out_specs=out_specs, check_vma=False
    )
```

```python
import jax
import jax.numpy as jnp
from jax import lax
from jax.sharding import PartitionSpec as P


def elu_plus(v):
    return jnp.where(v > 0, v + 1.0, jnp.exp(jnp.minimum(v, 0.0)))


def swap(x, axis, size, flip):
    return lax.ppermute(x, axis, [(i, i ^ flip) for i in range(size)])


def per_device(tokens, w_query, w_key, w_value, memory_in, norm_in, gate_logit):
    n_heads_dev = 4
    me = lax.axis_index("heads")
    n_seq = lax.axis_size("seq")
    place = lax.axis_index("seq")
    batch, seglen, part = tokens.shape
    kv_heads = memory_in.shape[1]
    head_size = memory_in.shape[2]
    q_heads = gate_logit.shape[0]
    group = q_heads // kv_heads
    qcols = w_query.shape[1]
    kcols = w_key.shape[1]
    width = group * head_size

    wall = jnp.concatenate([w_query, w_key, w_value], axis=1)
    wall = lax.all_gather(wall, "seq", axis=0, tiled=True)

    flat = tokens.reshape(batch * seglen, part)
    cross = swap(flat, "heads", n_heads_dev, 2)
    near = swap(flat, "heads", n_heads_dev, 1)
    far = swap(cross, "heads", n_heads_dev, 1)
    blocks = (flat, near, cross, far)
    full = jnp.zeros((batch * seglen, n_heads_dev * part), flat.dtype)
    for k, blk in enumerate(blocks):
        full = lax.dynamic_update_slice(full, blk, (0, (me ^ k) * part))
    zero = me // n_heads_dev

    def project(lo, hi):
        rows = lax.dynamic_slice(wall, (zero, lo + zero), (wall.shape[0], hi - lo))
        return jnp.dot(full, rows, preferred_element_type=jnp.float32).astype(jnp.bfloat16)

    kv = project(qcols, wall.shape[1])
    keys = kv[:, :kcols].reshape(seglen, kv_heads, head_size)
    values = kv[:, kcols:].reshape(seglen, kv_heads, head_size)
    highest = lax.Precision.HIGHEST
    sk = elu_plus(keys.astype(jnp.float32))
    contrib = jnp.einsum("sgi,sgj->gij", sk, values.astype(jnp.float32), precision=highest)
    zterm = jnp.sum(sk, axis=0)
    packed = jnp.concatenate([contrib.reshape(-1), zterm.reshape(-1)]).astype(jnp.bfloat16)
    packed, wall = lax.optimization_barrier((packed, wall))
    every = lax.all_gather(packed, "seq", axis=0, tiled=False)

    queries = project(0, qcols).reshape(seglen, kv_heads, group, head_size)
    scale = 1.0 / head_size**0.5
    causal = jnp.arange(seglen)[:, None] >= jnp.arange(seglen)[None, :]
    shares = jax.nn.sigmoid(gate_logit).reshape(kv_heads, group)

    locals_ = []
    for g in range(kv_heads):
        q_one = queries[:, g]
        scores = jnp.einsum("srd,td->rst", q_one, keys[:, g], preferred_element_type=jnp.float32) * scale
        scores = jnp.where(causal, scores, -jnp.inf)
        top = jnp.max(scores, axis=-1, keepdims=True)
        expo = jnp.exp(scores - top)
        weights = (expo / jnp.sum(expo, axis=-1, keepdims=True)).astype(jnp.bfloat16)
        locals_.append(jnp.einsum("rst,td->srd", weights, values[:, g], preferred_element_type=jnp.float32))

    every, locals_ = lax.optimization_barrier((every, locals_))
    mask = (jnp.arange(n_seq) < place).astype(jnp.float32)
    before = jnp.einsum("s,sn->n", mask, every.astype(jnp.float32), precision=highest)
    nmem = contrib.size
    memory = memory_in[0] + before[:nmem].reshape(contrib.shape)
    znorm = norm_in[0] + before[nmem:].reshape(zterm.shape)

    outs = []
    for g in range(kv_heads):
        sq = elu_plus(queries[:, g].astype(jnp.float32))
        numer = jnp.einsum("sri,ij->srj", sq, memory[g], precision=lax.Precision.HIGH)
        denom = jnp.einsum("sri,i->sr", sq, znorm[g], precision=lax.Precision.HIGH)
        retrieved = numer / denom[..., None]
        share = shares[g][None, :, None]
        outs.append((share * retrieved + (1.0 - share) * locals_[g]).astype(jnp.bfloat16).reshape(seglen, width))
    mixed = jnp.concatenate(outs, axis=1)
    return mixed.reshape(batch, seglen, q_heads * head_size)


def solution(mesh):
    in_specs = (
        P(None, "seq", "heads"),
        P("seq", "heads"),
        P("seq", "heads"),
        P("seq", "heads"),
        P(None, "heads", None, None),
        P(None, "heads", None),
        P("heads"),
    )
    out_specs = P(None, "seq", "heads")
    return jax.shard_map(
        per_device, mesh=mesh, in_specs=in_specs, out_specs=out_specs, check_vma=False
    )
```

```python
import jax
import jax.numpy as jnp
from jax import lax
from jax.sharding import PartitionSpec as P


def elu_plus(v):
    return jnp.where(v > 0, v + 1.0, jnp.exp(jnp.minimum(v, 0.0)))


def swap(x, axis, size, flip):
    return lax.ppermute(x, axis, [(i, i ^ flip) for i in range(size)])


def per_device(tokens, w_query, w_key, w_value, memory_in, norm_in, gate_logit):
    n_heads_dev = 4
    me = lax.axis_index("heads")
    n_seq = lax.axis_size("seq")
    place = lax.axis_index("seq")
    batch, seglen, part = tokens.shape
    kv_heads = memory_in.shape[1]
    head_size = memory_in.shape[2]
    q_heads = gate_logit.shape[0]
    group = q_heads // kv_heads
    qcols = w_query.shape[1]
    kcols = w_key.shape[1]

    wall = jnp.concatenate([w_query, w_key, w_value], axis=1)
    wall = lax.all_gather(wall, "seq", axis=0, tiled=True)

    flat = tokens.reshape(batch * seglen, part)
    cross = swap(flat, "heads", n_heads_dev, 2)
    near = swap(flat, "heads", n_heads_dev, 1)
    far = swap(cross, "heads", n_heads_dev, 1)
    blocks = (flat, near, cross, far)
    full = jnp.zeros((batch * seglen, n_heads_dev * part), flat.dtype)
    for k, blk in enumerate(blocks):
        full = lax.dynamic_update_slice(full, blk, (0, (me ^ k) * part))
    zero = me // n_heads_dev

    def project(lo, hi):
        rows = lax.dynamic_slice(wall, (zero, lo + zero), (wall.shape[0], hi - lo))
        return jnp.dot(full, rows, preferred_element_type=jnp.float32).astype(jnp.bfloat16)

    kv = project(qcols, wall.shape[1])
    keys = kv[:, :kcols].reshape(seglen, kv_heads, head_size)
    values = kv[:, kcols:].reshape(seglen, kv_heads, head_size)
    highest = lax.Precision.HIGHEST
    sk = elu_plus(keys.astype(jnp.float32))
    contrib = jnp.einsum("sgi,sgj->gij", sk, values.astype(jnp.float32), precision=highest)
    zterm = jnp.sum(sk, axis=0)
    packed = jnp.concatenate([contrib.reshape(-1), zterm.reshape(-1)]).astype(jnp.bfloat16)
    packed, wall = lax.optimization_barrier((packed, wall))
    every = lax.all_gather(packed.reshape(-1, 128), "seq", axis=0, tiled=False)

    queries = project(0, qcols).reshape(seglen, kv_heads, group, head_size)
    scale = 1.0 / head_size**0.5
    causal = jnp.arange(seglen)[:, None] >= jnp.arange(seglen)[None, :]
    shares = jax.nn.sigmoid(gate_logit).reshape(kv_heads, group)

    locals_ = []
    for g in range(kv_heads):
        q_one = queries[:, g]
        scores = jnp.einsum("srd,td->rst", q_one, keys[:, g], preferred_element_type=jnp.float32) * scale
        scores = jnp.where(causal, scores, -jnp.inf)
        top = jnp.max(scores, axis=-1, keepdims=True)
        expo = jnp.exp(scores - top)
        weights = (expo / jnp.sum(expo, axis=-1, keepdims=True)).astype(jnp.bfloat16)
        locals_.append(jnp.einsum("rst,td->srd", weights, values[:, g], preferred_element_type=jnp.float32))

    every, locals_ = lax.optimization_barrier((every, locals_))
    mask = (jnp.arange(n_seq) < place).astype(jnp.float32)
    before = jnp.sum(jnp.where(mask[:, None, None] > 0, every.astype(jnp.float32), 0.0), axis=0).reshape(-1)
    nmem = contrib.size
    memory = memory_in[0] + before[:nmem].reshape(contrib.shape)
    znorm = norm_in[0] + before[nmem:].reshape(zterm.shape)

    outs = []
    for g in range(kv_heads):
        sq = elu_plus(queries[:, g].astype(jnp.float32))
        numer = jnp.einsum("sri,ij->srj", sq, memory[g], precision=lax.Precision.HIGH)
        denom = jnp.einsum("sri,i->sr", sq, znorm[g], precision=lax.Precision.HIGH)
        retrieved = numer / denom[..., None]
        share = shares[g][None, :, None]
        outs.append((share * retrieved + (1.0 - share) * locals_[g]).astype(jnp.bfloat16))
    mixed = jnp.stack(outs, axis=1)
    return mixed.reshape(batch, seglen, q_heads * head_size)


def solution(mesh):
    in_specs = (
        P(None, "seq", "heads"),
        P("seq", "heads"),
        P("seq", "heads"),
        P("seq", "heads"),
        P(None, "heads", None, None),
        P(None, "heads", None),
        P("heads"),
    )
    out_specs = P(None, "seq", "heads")
    return jax.shard_map(
        per_device, mesh=mesh, in_specs=in_specs, out_specs=out_specs, check_vma=False
    )
```

```python
import jax
import jax.numpy as jnp
from jax import lax
from jax.sharding import PartitionSpec as P


def elu_plus(v):
    return jnp.where(v > 0, v + 1.0, jnp.exp(jnp.minimum(v, 0.0)))


def swap(x, axis, size, flip):
    return lax.ppermute(x, axis, [(i, i ^ flip) for i in range(size)])


def per_device(tokens, w_query, w_key, w_value, memory_in, norm_in, gate_logit):
    n_heads_dev = 4
    me = lax.axis_index("heads")
    n_seq = lax.axis_size("seq")
    place = lax.axis_index("seq")
    batch, seglen, part = tokens.shape
    kv_heads = memory_in.shape[1]
    head_size = memory_in.shape[2]
    q_heads = gate_logit.shape[0]
    group = q_heads // kv_heads
    qcols = w_query.shape[1]
    kcols = w_key.shape[1]

    wall = jnp.concatenate([w_query, w_key, w_value], axis=1)
    wall = lax.all_gather(wall, "seq", axis=0, tiled=True)

    flat = tokens.reshape(batch * seglen, part)
    cross = swap(flat, "heads", n_heads_dev, 2)
    near = swap(flat, "heads", n_heads_dev, 1)
    far = swap(cross, "heads", n_heads_dev, 1)
    blocks = (flat, near, cross, far)
    full = jnp.zeros((batch * seglen, n_heads_dev * part), flat.dtype)
    for k, blk in enumerate(blocks):
        full = lax.dynamic_update_slice(full, blk, (0, (me ^ k) * part))
    zero = me // n_heads_dev

    def project(lo, hi):
        rows = lax.dynamic_slice(wall, (zero, lo + zero), (wall.shape[0], hi - lo))
        return jnp.dot(full, rows, preferred_element_type=jnp.float32).astype(jnp.bfloat16)

    kv = project(qcols, wall.shape[1])
    keys = kv[:, :kcols].reshape(seglen, kv_heads, head_size)
    values = kv[:, kcols:].reshape(seglen, kv_heads, head_size)
    highest = lax.Precision.HIGHEST
    sk = elu_plus(keys.astype(jnp.float32))
    contrib = jnp.einsum("sgi,sgj->gij", sk, values.astype(jnp.float32), precision=highest)
    zterm = jnp.sum(sk, axis=0)
    packed = jnp.concatenate([contrib.reshape(-1), zterm.reshape(-1)]).astype(jnp.bfloat16)
    packed, wall = lax.optimization_barrier((packed, wall))
    every = lax.all_gather(packed.reshape(-1, 128), "seq", axis=0, tiled=False)

    queries = project(0, qcols).reshape(seglen, kv_heads, group, head_size)
    scale = 1.0 / head_size**0.5
    causal = jnp.arange(seglen)[:, None] >= jnp.arange(seglen)[None, :]
    shares = jax.nn.sigmoid(gate_logit).reshape(kv_heads, group)

    locals_ = []
    for g in range(kv_heads):
        q_one = queries[:, g]
        scores = jnp.einsum("srd,td->rst", q_one, keys[:, g], preferred_element_type=jnp.float32) * scale
        scores = jnp.where(causal, scores, -jnp.inf)
        top = jnp.max(scores, axis=-1, keepdims=True)
        expo = jnp.exp(scores - top)
        weights = (expo / jnp.sum(expo, axis=-1, keepdims=True)).astype(jnp.bfloat16)
        locals_.append(jnp.einsum("rst,td->srd", weights, values[:, g], preferred_element_type=jnp.float32))

    every, locals_ = lax.optimization_barrier((every, locals_))
    mask = (jnp.arange(n_seq) < place).astype(jnp.float32)
    before = jnp.sum(jnp.where(mask[:, None, None] > 0, every.astype(jnp.float32), 0.0), axis=0).reshape(-1)
    nmem = contrib.size
    memory = memory_in[0] + before[:nmem].reshape(contrib.shape)
    znorm = norm_in[0] + before[nmem:].reshape(zterm.shape)

    outs = []
    for g in range(kv_heads):
        sq = elu_plus(queries[:, g].astype(jnp.float32))
        numer = jnp.einsum("sri,ij->srj", sq, memory[g], preferred_element_type=jnp.float32)
        denom = jnp.einsum("sri,i->sr", sq, znorm[g], preferred_element_type=jnp.float32)
        retrieved = numer / denom[..., None]
        share = shares[g][None, :, None]
        outs.append((share * retrieved + (1.0 - share) * locals_[g]).astype(jnp.bfloat16))
    mixed = jnp.stack(outs, axis=1)
    return mixed.reshape(batch, seglen, q_heads * head_size)


def solution(mesh):
    in_specs = (
        P(None, "seq", "heads"),
        P("seq", "heads"),
        P("seq", "heads"),
        P("seq", "heads"),
        P(None, "heads", None, None),
        P(None, "heads", None),
        P("heads"),
    )
    out_specs = P(None, "seq", "heads")
    return jax.shard_map(
        per_device, mesh=mesh, in_specs=in_specs, out_specs=out_specs, check_vma=False
    )
```
